256 devices in a mesh: tm: 32 (over y, z_hi, core), rows: 8 (over z_lo, x).
Axes of the slice: x: 4, y: 4, z: 8 (z_hi: 4, z_lo: 2; z = z_hi * 2 + z_lo), core: 2. Of those that a mesh axis runs over, the one named last changes fastest.
Arguments:
- latent: bfloat16 [32, 16, 128, 512], P('tm', 'rows'), may hold values from -32 to 32
- norm_gain: float32 [512], replicated, may hold values from 0.1 to 1.9
- conv_weight: bfloat16 [27, 512, 512], P(None, 'tm'), may hold values from -0.0546875 to 0.0546875
- grad_out: bfloat16 [32, 16, 128, 512], P('tm', 'rows'), may hold values from -6 to 6
Outputs:
- refined: bfloat16 [32, 16, 128, 512], P('tm', 'rows')
- grad_latent: float32 [32, 16, 128, 512], P('tm', 'rows')
The draws below stay inside these ranges and needn't reach their ends.
All inputs are finite; a program needn't handle non-finite values.
Results may differ from the reference program's by a relative error of at most 0.0013.
The reference program's roundings to bfloat16 on the way (of `activated`) count: a program that leaves them out, or rounds other values in their place, can miss the bound.
Values may be sent and summed in bfloat16 or wider, within the bound.
No kernel may reach another device: no remote copies, remote signals or barrier semaphores. Data moves between devices by JAX's collectives and lax.ppermute only.
A program may use at most 64 MiB of HBM per device.

```python
import jax
import jax.numpy as jnp
from jax import lax

C = 512
GROUPS = 32
TAPS = 27
COLS = 128
FRAMES = 32
HEIGHT = 16


def draw_latent(key, part):
    key_mean, key_rough, key_noise = jax.random.split(key, 3)
    positions = jnp.arange(HEIGHT, dtype=jnp.float32) / max(HEIGHT - 1, 1)
    channel_mean = jnp.clip(jax.random.normal(key_mean, (C,), jnp.float32), -4.0, 4.0)
    rough = jnp.exp(jax.random.uniform(key_rough, (FRAMES, HEIGHT, COLS, 1), jnp.float32, -0.7, 0.7))
    rise = 1.0 + 2.0 * positions
    noise = jnp.clip(jax.random.normal(key_noise, (FRAMES, HEIGHT, COLS, C), jnp.float32), -4.0, 4.0)
    values = rise[None, :, None, None] * (0.5 * channel_mean + noise * rough)
    return jnp.clip(values, -32.0, 32.0).astype(jnp.bfloat16)


def level_of(rng, extent, cuts, low, top_value):
    factor_of, own = 1.0, jax.random.fold_in(rng, 6)
    for position, blocks in cuts:
        draws = jnp.exp(jax.random.uniform(jax.random.fold_in(own, position), (blocks,), jnp.float32, low / len(cuts), top_value / len(cuts)))
        factor_of = factor_of * jnp.repeat(draws, extent[position] // blocks).reshape([-1 if axis == position else 1 for axis in range(len(extent))])
    return factor_of


def normal_values(key, dims, deviation, most, shards=(), kind=jnp.bfloat16):
    entries = jax.random.normal(key, dims, jnp.float32) * deviation
    if len(shards) > 0:
        entries = level_of(key, dims, shards, -0.22, 0.18) * entries
    return jnp.clip(entries, min=-most, max=most).astype(kind)


def setup_inputs(seed: int = 0) -> dict:
    key_list = jax.random.split(jax.random.key(seed), 5)
    latent = draw_latent(jax.random.fold_in(key_list[4], 71), 0)
    norm_gain = jnp.clip(1.0 + 0.18 * jax.random.normal(key_list[1], (C,), jnp.float32), 0.1, 1.9)
    conv_weight = normal_values(key_list[2], (TAPS, C, C), (TAPS * C) ** -0.5, 0.0546875, ((1, 32),))
    grad_out = normal_values(key_list[3], (FRAMES, HEIGHT, COLS, C), 1.0, 6.0, ((0, 32), (1, 8)))
    return dict(latent=latent, norm_gain=norm_gain, conv_weight=conv_weight, grad_out=grad_out)


epsilon = 1e-06

def grouped_view(values):
    return values.reshape(values.shape[0], values.shape[1] * values.shape[2], GROUPS, values.shape[3] // GROUPS)

def reference(latent, norm_gain, conv_weight, grad_out):
    frames_all, height_all, columns, channels = latent.shape
    cell_count = height_all * columns * (channels // GROUPS)
    latent_wide = latent.astype(jnp.float32)
    grouped = grouped_view(latent_wide)
    average = lax.optimization_barrier(jnp.sum(grouped, axis=(1, 3))) / cell_count
    centred = grouped - average[:, None, :, None]
    spread = lax.optimization_barrier(jnp.sum(centred * centred, axis=(1, 3))) / cell_count
    inverse = lax.rsqrt(spread + epsilon)
    normed_grouped = centred * inverse[:, None, :, None]
    normed = normed_grouped.reshape(latent.shape)
    gain_wide = norm_gain.astype(jnp.float32)
    scaled = normed * gain_wide
    sigmoid_value = jax.nn.sigmoid(scaled)
    activated = (scaled * sigmoid_value).astype(jnp.bfloat16)
    weight_wide = conv_weight.astype(jnp.float32)
    padded = jnp.pad(activated, ((2, 0), (1, 1), (1, 1), (0, 0)))
    conv_sum = jnp.zeros((frames_all * height_all * columns, channels), jnp.float32)
    for time_tap in range(3):
        for row_tap in range(3):
            for col_tap in range(3):
                window = padded[time_tap:time_tap + frames_all, row_tap:row_tap + height_all, col_tap:col_tap + columns]
                conv_sum = conv_sum + jnp.dot(window.reshape(-1, channels).astype(jnp.float32), weight_wide[time_tap * 9 + row_tap * 3 + col_tap], preferred_element_type=jnp.float32)
    refined = (latent_wide + conv_sum.reshape(latent.shape)).astype(jnp.bfloat16)
    padded_grad = jnp.pad(grad_out, ((0, 2), (1, 1), (1, 1), (0, 0)))
    grad_act = jnp.zeros((frames_all * height_all * columns, channels), jnp.float32)
    for time_tap in range(3):
        for row_tap in range(3):
            for col_tap in range(3):
                window = padded_grad[2 - time_tap:2 - time_tap + frames_all, 2 - row_tap:2 - row_tap + height_all, 2 - col_tap:2 - col_tap + columns]
                grad_act = grad_act + jnp.dot(window.reshape(-1, channels).astype(jnp.float32), weight_wide[time_tap * 9 + row_tap * 3 + col_tap].T, preferred_element_type=jnp.float32)
    grad_scaled = grad_act.reshape(latent.shape) * sigmoid_value * (1.0 + scaled * (1.0 - sigmoid_value))
    grad_normed = grouped_view(grad_scaled * gain_wide)
    first = lax.optimization_barrier(jnp.sum(grad_normed, axis=(1, 3))) / cell_count
    second = lax.optimization_barrier(jnp.sum(grad_normed * normed_grouped, axis=(1, 3))) / cell_count
    grad_norm_part = (grad_normed - first[:, None, :, None] - normed_grouped * second[:, None, :, None]) * inverse[:, None, :, None]
    grad_latent = grad_out.astype(jnp.float32) + grad_norm_part.reshape(latent.shape)
    return (refined, grad_latent)
```

```python
import jax
import jax.numpy as jnp
from jax import lax
from jax.sharding import PartitionSpec as P

GROUPS = 32


epsilon = 1e-06


def shifted(block, axis, distance):
    devices = range(lax.axis_size(axis))
    route = [(i - distance, i) for i in devices if i - distance in devices]
    return lax.ppermute(block, axis, route)


def with_halo(shard, sides, width):
    for axis, dim in sides:
        size, length = (lax.axis_size(axis), shard.shape[dim])
        up = [(i, (i + 1) % size) for i in range(size - 1)]
        down = [(j, i) for i, j in up]
        last = lax.slice_in_dim(shard, length - width, length, axis=dim)
        first = lax.slice_in_dim(shard, 0, width, axis=dim)
        before = lax.ppermute(last, axis, up)
        after = lax.ppermute(first, axis, down)
        shard = jnp.concatenate([before, shard, after], axis=dim)
    return shard


def grouped_view(values):
    return values.reshape(
        values.shape[0], values.shape[1] * values.shape[2], GROUPS, values.shape[3] // GROUPS
    )


def widen_columns(values):
    return jnp.pad(values, ((0, 0), (0, 0), (1, 1), (0, 0)))


def plane_windows(plane, rows_here, columns, flip):
    taps = []
    for row_tap in range(3):
        for col_tap in range(3):
            r0 = 2 - row_tap if flip else row_tap
            c0 = 2 - col_tap if flip else col_tap
            window = plane[r0 : r0 + rows_here, c0 : c0 + columns]
            taps.append(window.reshape(rows_here * columns, 1, plane.shape[-1]))
    return jnp.concatenate(taps, axis=1)


def shards(latent, norm_gain, conv_weight, grad_out):
    frames_here, rows_here, columns, channels = latent.shape
    cell_count = lax.axis_size("rows") * rows_here * columns * (channels // GROUPS)
    weight_parts = [
        lax.all_gather(conv_weight[9 * a : 9 * a + 9], "tm", axis=1, tiled=True) for a in range(3)
    ]
    after_one = shifted(grad_out, "tm", -1)
    after_two = shifted(grad_out, "tm", -2)
    padded_grad = with_halo(
        jnp.concatenate([grad_out, after_one, after_two], axis=0), (("rows", 1),), 1
    )
    padded_grad = widen_columns(padded_grad)
    latent_wide = latent.astype(jnp.float32)
    grouped = grouped_view(latent_wide)
    average = lax.psum(jnp.sum(grouped, axis=(1, 3)), "rows") / cell_count
    centred = grouped - average[:, None, :, None]
    spread = lax.psum(jnp.sum(centred * centred, axis=(1, 3)), "rows") / cell_count
    inverse = lax.rsqrt(spread + epsilon)
    normed_grouped = centred * inverse[:, None, :, None]
    normed = normed_grouped.reshape(latent.shape)
    scaled = normed * norm_gain
    sigmoid_value = jax.nn.sigmoid(scaled)
    activated = (scaled * sigmoid_value).astype(jnp.bfloat16)
    before_one = shifted(activated, "tm", 1)
    before_two = shifted(activated, "tm", 2)
    padded = with_halo(
        jnp.concatenate([before_two, before_one, activated], axis=0), (("rows", 1),), 1
    )
    padded = widen_columns(padded)
    positions = frames_here * rows_here * columns
    grad_act = None
    conv_sum = None
    for time_tap in range(3):
        part = weight_parts[time_tap]
        if time_tap > 0:
            part, grad_act, conv_sum = lax.optimization_barrier((part, grad_act, conv_sum))
        back = plane_windows(padded_grad[2 - time_tap], rows_here, columns, True)
        term = lax.dot_general(
            back, part, (((1, 2), (0, 2)), ((), ())), preferred_element_type=jnp.float32
        )
        grad_act = term if grad_act is None else grad_act + term
        fwd = plane_windows(padded[time_tap], rows_here, columns, False)
        term = jnp.dot(
            fwd.reshape(positions, 9 * channels),
            part.reshape(9 * channels, channels),
            preferred_element_type=jnp.float32,
        )
        conv_sum = term if conv_sum is None else conv_sum + term
    grad_scaled = (
        grad_act.reshape(latent.shape) * sigmoid_value * (1.0 + scaled * (1.0 - sigmoid_value))
    )
    grad_normed = grouped_view(grad_scaled * norm_gain)
    partial = jnp.stack(
        [jnp.sum(grad_normed, axis=(1, 3)), jnp.sum(grad_normed * normed_grouped, axis=(1, 3))]
    )
    size = lax.axis_size("rows")
    total = partial
    for distance in range(1, size):
        total = total + lax.ppermute(partial, "rows", [(i, (i + distance) % size) for i in range(size)])
    first_sum, second_sum = total
    refined = (latent_wide + conv_sum.reshape(latent.shape)).astype(jnp.bfloat16)
    first = first_sum / cell_count
    second = second_sum / cell_count
    grad_norm_part = (
        grad_normed - first[:, None, :, None] - normed_grouped * second[:, None, :, None]
    ) * inverse[:, None, :, None]
    grad_latent = grad_out.astype(jnp.float32) + grad_norm_part.reshape(latent.shape)
    return (refined, grad_latent)


def solution(mesh):
    placed = (P("tm", "rows", None, None), P(), P(None, "tm", None), P("tm", "rows", None, None))
    return jax.shard_map(
        shards,
        mesh=mesh,
        in_specs=placed,
        out_specs=(P("tm", "rows", None, None), P("tm", "rows", None, None)),
        check_vma=False,
    )
```

```python
import jax
import jax.numpy as jnp
from jax import lax
from jax.sharding import PartitionSpec as P

GROUPS = 32


epsilon = 1e-06


def shifted(block, axis, distance):
    devices = range(lax.axis_size(axis))
    route = [(i - distance, i) for i in devices if i - distance in devices]
    return lax.ppermute(block, axis, route)


def with_halo(shard, sides, width):
    for axis, dim in sides:
        size, length = (lax.axis_size(axis), shard.shape[dim])
        up = [(i, (i + 1) % size) for i in range(size - 1)]
        down = [(j, i) for i, j in up]
        last = lax.slice_in_dim(shard, length - width, length, axis=dim)
        first = lax.slice_in_dim(shard, 0, width, axis=dim)
        before = lax.ppermute(last, axis, up)
        after = lax.ppermute(first, axis, down)
        shard = jnp.concatenate([before, shard, after], axis=dim)
    return shard


def grouped_view(values):
    return values.reshape(
        values.shape[0], values.shape[1] * values.shape[2], GROUPS, values.shape[3] // GROUPS
    )


def widen_columns(values):
    return jnp.pad(values, ((0, 0), (0, 0), (1, 1), (0, 0)))


def plane_windows(plane, rows_here, columns, flip):
    taps = []
    for row_tap in range(3):
        for col_tap in range(3):
            r0 = 2 - row_tap if flip else row_tap
            c0 = 2 - col_tap if flip else col_tap
            window = plane[r0 : r0 + rows_here, c0 : c0 + columns]
            taps.append(window.reshape(rows_here * columns, 1, plane.shape[-1]))
    return jnp.concatenate(taps, axis=1)


def shards(latent, norm_gain, conv_weight, grad_out):
    frames_here, rows_here, columns, channels = latent.shape
    cell_count = lax.axis_size("rows") * rows_here * columns * (channels // GROUPS)
    full_weight = lax.all_gather(conv_weight, "tm", axis=1, tiled=True)
    after_one = shifted(grad_out, "tm", -1)
    after_two = shifted(grad_out, "tm", -2)
    padded_grad = with_halo(
        jnp.concatenate([grad_out, after_one, after_two], axis=0), (("rows", 1),), 1
    )
    padded_grad = widen_columns(padded_grad)
    latent_wide = latent.astype(jnp.float32)
    grouped = grouped_view(latent_wide)
    average = lax.psum(jnp.sum(grouped, axis=(1, 3)), "rows") / cell_count
    centred = grouped - average[:, None, :, None]
    spread = lax.psum(jnp.sum(centred * centred, axis=(1, 3)), "rows") / cell_count
    inverse = lax.rsqrt(spread + epsilon)
    normed_grouped = centred * inverse[:, None, :, None]
    normed = normed_grouped.reshape(latent.shape)
    scaled = normed * norm_gain
    sigmoid_value = jax.nn.sigmoid(scaled)
    activated = (scaled * sigmoid_value).astype(jnp.bfloat16)
    before_one = shifted(activated, "tm", 1)
    before_two = shifted(activated, "tm", 2)
    padded = with_halo(
        jnp.concatenate([before_two, before_one, activated], axis=0), (("rows", 1),), 1
    )
    padded = widen_columns(padded)
    positions = frames_here * rows_here * columns
    full_weight, padded, padded_grad = lax.optimization_barrier((full_weight, padded, padded_grad))
    grad_act = None
    for time_tap in range(3):
        part = full_weight[9 * time_tap : 9 * time_tap + 9]
        back = plane_windows(padded_grad[2 - time_tap], rows_here, columns, True)
        term = lax.dot_general(
            back, part, (((1, 2), (0, 2)), ((), ())), preferred_element_type=jnp.float32
        )
        grad_act = term if grad_act is None else grad_act + term
    grad_scaled = (
        grad_act.reshape(latent.shape) * sigmoid_value * (1.0 + scaled * (1.0 - sigmoid_value))
    )
    grad_normed = grouped_view(grad_scaled * norm_gain)
    partial = jnp.stack(
        [jnp.sum(grad_normed, axis=(1, 3)), jnp.sum(grad_normed * normed_grouped, axis=(1, 3))]
    )
    full_weight, padded, partial = lax.optimization_barrier((full_weight, padded, partial))
    size = lax.axis_size("rows")
    total = partial
    for distance in range(1, size):
        total = total + lax.ppermute(partial, "rows", [(i, (i + distance) % size) for i in range(size)])
    first_sum, second_sum = total
    conv_sum = None
    for time_tap in range(3):
        part = full_weight[9 * time_tap : 9 * time_tap + 9]
        fwd = plane_windows(padded[time_tap], rows_here, columns, False)
        term = jnp.dot(
            fwd.reshape(positions, 9 * channels),
            part.reshape(9 * channels, channels),
            preferred_element_type=jnp.float32,
        )
        conv_sum = term if conv_sum is None else conv_sum + term
    refined = (latent_wide + conv_sum.reshape(latent.shape)).astype(jnp.bfloat16)
    first = first_sum / cell_count
    second = second_sum / cell_count
    grad_norm_part = (
        grad_normed - first[:, None, :, None] - normed_grouped * second[:, None, :, None]
    ) * inverse[:, None, :, None]
    grad_latent = grad_out.astype(jnp.float32) + grad_norm_part.reshape(latent.shape)
    return (refined, grad_latent)


def solution(mesh):
    placed = (P("tm", "rows", None, None), P(), P(None, "tm", None), P("tm", "rows", None, None))
    return jax.shard_map(
        shards,
        mesh=mesh,
        in_specs=placed,
        out_specs=(P("tm", "rows", None, None), P("tm", "rows", None, None)),
        check_vma=False,
    )
```

```python
import jax
import jax.numpy as jnp
from jax import lax
from jax.sharding import PartitionSpec as P

GROUPS = 32


epsilon = 1e-06


def shifted(block, axis, distance):
    devices = range(lax.axis_size(axis))
    route = [(i - distance, i) for i in devices if i - distance in devices]
    return lax.ppermute(block, axis, route)


def with_halo(shard, sides, width):
    for axis, dim in sides:
        size, length = (lax.axis_size(axis), shard.shape[dim])
        up = [(i, (i + 1) % size) for i in range(size - 1)]
        down = [(j, i) for i, j in up]
        last = lax.slice_in_dim(shard, length - width, length, axis=dim)
        first = lax.slice_in_dim(shard, 0, width, axis=dim)
        before = lax.ppermute(last, axis, up)
        after = lax.ppermute(first, axis, down)
        shard = jnp.concatenate([before, shard, after], axis=dim)
    return shard


def grouped_view(values):
    return values.reshape(
        values.shape[0], values.shape[1] * values.shape[2], GROUPS, values.shape[3] // GROUPS
    )


def widen_columns(values):
    return jnp.pad(values, ((0, 0), (0, 0), (1, 1), (0, 0)))


def plane_windows(plane, rows_here, columns, flip):
    taps = []
    for row_tap in range(3):
        for col_tap in range(3):
            r0 = 2 - row_tap if flip else row_tap
            c0 = 2 - col_tap if flip else col_tap
            window = plane[r0 : r0 + rows_here, c0 : c0 + columns]
            taps.append(window.reshape(rows_here * columns, 1, plane.shape[-1]))
    return jnp.concatenate(taps, axis=1)


def shards(latent, norm_gain, conv_weight, grad_out):
    frames_here, rows_here, columns, channels = latent.shape
    cell_count = lax.axis_size("rows") * rows_here * columns * (channels // GROUPS)
    full_weight = lax.all_gather(conv_weight, "tm", axis=1, tiled=True)
    after_one = shifted(grad_out, "tm", -1)
    after_two = shifted(grad_out, "tm", -2)
    padded_grad = with_halo(
        jnp.concatenate([grad_out, after_one, after_two], axis=0), (("rows", 1),), 1
    )
    padded_grad = widen_columns(padded_grad)
    latent_block = jnp.concatenate(
        [shifted(latent, "tm", 2), shifted(latent, "tm", 1), latent], axis=0
    )
    latent_padded = with_halo(latent_block, (("rows", 1),), 1)
    latent_wide = latent.astype(jnp.float32)
    grouped_block = grouped_view(latent_block.astype(jnp.float32))
    average_block = lax.psum(jnp.sum(grouped_block, axis=(1, 3)), "rows") / cell_count
    centred_block = grouped_block - average_block[:, None, :, None]
    spread_block = (
        lax.psum(jnp.sum(centred_block * centred_block, axis=(1, 3)), "rows") / cell_count
    )
    inverse_block = lax.rsqrt(spread_block + epsilon)
    inverse = inverse_block[2:]
    normed_grouped = centred_block[2:] * inverse[:, None, :, None]
    normed = normed_grouped.reshape(latent.shape)
    scaled = normed * norm_gain
    sigmoid_value = jax.nn.sigmoid(scaled)
    wide_padded = grouped_view(latent_padded.astype(jnp.float32))
    normed_padded = (wide_padded - average_block[:, None, :, None]) * inverse_block[:, None, :, None]
    scaled_padded = normed_padded.reshape(latent_padded.shape) * norm_gain
    activated_padded = (scaled_padded * jax.nn.sigmoid(scaled_padded)).astype(jnp.bfloat16)
    frame_index = lax.axis_index("tm") * frames_here - 2 + lax.iota(jnp.int32, 3)
    row_index = lax.axis_index("rows") * rows_here - 1 + lax.iota(jnp.int32, rows_here + 2)
    inside = (frame_index[:, None] >= 0) & (row_index[None, :] >= 0)
    inside = inside & (row_index[None, :] < lax.axis_size("rows") * rows_here)
    padded = jnp.where(inside[:, :, None, None], activated_padded, jnp.zeros_like(activated_padded))
    padded = widen_columns(padded)
    positions = frames_here * rows_here * columns
    full_weight, padded, padded_grad = lax.optimization_barrier((full_weight, padded, padded_grad))
    grad_act = None
    for time_tap in range(3):
        part = full_weight[9 * time_tap : 9 * time_tap + 9]
        back = plane_windows(padded_grad[2 - time_tap], rows_here, columns, True)
        term = lax.dot_general(
            back, part, (((1, 2), (0, 2)), ((), ())), preferred_element_type=jnp.float32
        )
        grad_act = term if grad_act is None else grad_act + term
    grad_scaled = (
        grad_act.reshape(latent.shape) * sigmoid_value * (1.0 + scaled * (1.0 - sigmoid_value))
    )
    grad_normed = grouped_view(grad_scaled * norm_gain)
    partial = jnp.stack(
        [jnp.sum(grad_normed, axis=(1, 3)), jnp.sum(grad_normed * normed_grouped, axis=(1, 3))]
    )
    full_weight, padded, partial = lax.optimization_barrier((full_weight, padded, partial))
    size = lax.axis_size("rows")
    total = partial
    for distance in range(1, size):
        total = total + lax.ppermute(partial, "rows", [(i, (i + distance) % size) for i in range(size)])
    first_sum, second_sum = total
    conv_sum = None
    for time_tap in range(3):
        part = full_weight[9 * time_tap : 9 * time_tap + 9]
        fwd = plane_windows(padded[time_tap], rows_here, columns, False)
        term = jnp.dot(
            fwd.reshape(positions, 9 * channels),
            part.reshape(9 * channels, channels),
            preferred_element_type=jnp.float32,
        )
        conv_sum = term if conv_sum is None else conv_sum + term
    refined = (latent_wide + conv_sum.reshape(latent.shape)).astype(jnp.bfloat16)
    first = first_sum / cell_count
    second = second_sum / cell_count
    grad_norm_part = (
        grad_normed - first[:, None, :, None] - normed_grouped * second[:, None, :, None]
    ) * inverse[:, None, :, None]
    grad_latent = grad_out.astype(jnp.float32) + grad_norm_part.reshape(latent.shape)
    return (refined, grad_latent)


def solution(mesh):
    placed = (P("tm", "rows", None, None), P(), P(None, "tm", None), P("tm", "rows", None, None))
    return jax.shard_map(
        shards,
        mesh=mesh,
        in_specs=placed,
        out_specs=(P("tm", "rows", None, None), P("tm", "rows", None, None)),
        check_vma=False,
    )
```

```python
import jax
import jax.numpy as jnp
from jax import lax
from jax.sharding import PartitionSpec as P

GROUPS = 32


epsilon = 1e-06


def shifted(block, axis, distance):
    devices = range(lax.axis_size(axis))
    route = [(i - distance, i) for i in devices if i - distance in devices]
    return lax.ppermute(block, axis, route)


def with_halo(shard, sides, width):
    for axis, dim in sides:
        size, length = (lax.axis_size(axis), shard.shape[dim])
        up = [(i, (i + 1) % size) for i in range(size - 1)]
        down = [(j, i) for i, j in up]
        last = lax.slice_in_dim(shard, length - width, length, axis=dim)
        first = lax.slice_in_dim(shard, 0, width, axis=dim)
        before = lax.ppermute(last, axis, up)
        after = lax.ppermute(first, axis, down)
        shard = jnp.concatenate([before, shard, after], axis=dim)
    return shard


def grouped_view(values):
    return values.reshape(
        values.shape[0], values.shape[1] * values.shape[2], GROUPS, values.shape[3] // GROUPS
    )


def group_sums(values):
    per = jnp.sum(values, axis=(1, 2))
    return jnp.sum(per.reshape(per.shape[0], GROUPS, per.shape[1] // GROUPS), axis=2)


def per_channel(stats, channels):
    wide = jnp.repeat(stats, channels // GROUPS, axis=1)
    return wide[:, None, None, :]


def widen_columns(values):
    return jnp.pad(values, ((0, 0), (0, 0), (1, 1), (0, 0)))


def plane_windows(plane, rows_here, columns, flip):
    taps = []
    for row_tap in range(3):
        for col_tap in range(3):
            r0 = 2 - row_tap if flip else row_tap
            c0 = 2 - col_tap if flip else col_tap
            window = plane[r0 : r0 + rows_here, c0 : c0 + columns]
            taps.append(window.reshape(rows_here * columns, 1, plane.shape[-1]))
    return jnp.concatenate(taps, axis=1)


def shards(latent, norm_gain, conv_weight, grad_out):
    frames_here, rows_here, columns, channels = latent.shape
    cell_count = lax.axis_size("rows") * rows_here * columns * (channels // GROUPS)
    full_weight = lax.all_gather(conv_weight, "tm", axis=1, tiled=True)
    after_one = shifted(grad_out, "tm", -1)
    after_two = shifted(grad_out, "tm", -2)
    padded_grad = with_halo(
        jnp.concatenate([grad_out, after_one, after_two], axis=0), (("rows", 1),), 1
    )
    padded_grad = widen_columns(padded_grad)
    latent_block = jnp.concatenate(
        [shifted(latent, "tm", 2), shifted(latent, "tm", 1), latent], axis=0
    )
    latent_padded = with_halo(latent_block, (("rows", 1),), 1)
    latent_wide = latent.astype(jnp.float32)
    block_wide = latent_block.astype(jnp.float32)
    average_block = lax.psum(group_sums(block_wide), "rows") / cell_count
    centred_block = block_wide - per_channel(average_block, channels)
    spread_block = lax.psum(group_sums(centred_block * centred_block), "rows") / cell_count
    inverse_block = lax.rsqrt(spread_block + epsilon)
    inverse = per_channel(inverse_block[2:], channels)
    normed = centred_block[2:] * inverse
    scaled = normed * norm_gain
    sigmoid_value = jax.nn.sigmoid(scaled)
    padded_average = per_channel(average_block, channels)
    padded_inverse = per_channel(inverse_block, channels)
    normed_padded = (latent_padded.astype(jnp.float32) - padded_average) * padded_inverse
    scaled_padded = normed_padded * norm_gain
    activated_padded = (scaled_padded * jax.nn.sigmoid(scaled_padded)).astype(jnp.bfloat16)
    frame_index = lax.axis_index("tm") * frames_here - 2 + lax.iota(jnp.int32, 3)
    row_index = lax.axis_index("rows") * rows_here - 1 + lax.iota(jnp.int32, rows_here + 2)
    inside = (frame_index[:, None] >= 0) & (row_index[None, :] >= 0)
    inside = inside & (row_index[None, :] < lax.axis_size("rows") * rows_here)
    padded = jnp.where(inside[:, :, None, None], activated_padded, jnp.zeros_like(activated_padded))
    padded = widen_columns(padded)
    positions = frames_here * rows_here * columns
    full_weight, padded, padded_grad = lax.optimization_barrier((full_weight, padded, padded_grad))
    grad_act = None
    for time_tap in range(3):
        part = full_weight[9 * time_tap : 9 * time_tap + 9]
        back = plane_windows(padded_grad[2 - time_tap], rows_here, columns, True)
        term = lax.dot_general(
            back, part, (((1, 2), (0, 2)), ((), ())), preferred_element_type=jnp.float32
        )
        grad_act = term if grad_act is None else grad_act + term
    grad_scaled = (
        grad_act.reshape(latent.shape) * sigmoid_value * (1.0 + scaled * (1.0 - sigmoid_value))
    )
    grad_normed = grad_scaled * norm_gain
    partial = jnp.stack([group_sums(grad_normed), group_sums(grad_normed * normed)])
    full_weight, padded, partial = lax.optimization_barrier((full_weight, padded, partial))
    size = lax.axis_size("rows")
    total = partial
    for distance in range(1, size):
        route = [(i, (i + distance) % size) for i in range(size)]
        total = total + lax.ppermute(partial, "rows", route)
    first_sum, second_sum = total
    conv_sum = None
    for time_tap in range(3):
        part = full_weight[9 * time_tap : 9 * time_tap + 9]
        fwd = plane_windows(padded[time_tap], rows_here, columns, False)
        term = jnp.dot(
            fwd.reshape(positions, 9 * channels),
            part.reshape(9 * channels, channels),
            preferred_element_type=jnp.float32,
        )
        conv_sum = term if conv_sum is None else conv_sum + term
    refined = (latent_wide + conv_sum.reshape(latent.shape)).astype(jnp.bfloat16)
    first = first_sum / cell_count
    second = second_sum / cell_count
    first_wide = per_channel(first, channels)
    second_wide = per_channel(second, channels)
    grad_norm_part = (grad_normed - first_wide - normed * second_wide) * inverse
    grad_latent = grad_out.astype(jnp.float32) + grad_norm_part
    return (refined, grad_latent)


def solution(mesh):
    placed = (P("tm", "rows", None, None), P(), P(None, "tm", None), P("tm", "rows", None, None))
    return jax.shard_map(
        shards,
        mesh=mesh,
        in_specs=placed,
        out_specs=(P("tm", "rows", None, None), P("tm", "rows", None, None)),
        check_vma=False,
    )
```

```python
import jax
import jax.numpy as jnp
from jax import lax
from jax.sharding import PartitionSpec as P

GROUPS = 32


epsilon = 1e-06


def shifted(block, axis, distance):
    devices = range(lax.axis_size(axis))
    route = [(i - distance, i) for i in devices if i - distance in devices]
    return lax.ppermute(block, axis, route)


def with_halo(shard, sides, width):
    for axis, dim in sides:
        size, length = (lax.axis_size(axis), shard.shape[dim])
        up = [(i, (i + 1) % size) for i in range(size - 1)]
        down = [(j, i) for i, j in up]
        last = lax.slice_in_dim(shard, length - width, length, axis=dim)
        first = lax.slice_in_dim(shard, 0, width, axis=dim)
        before = lax.ppermute(last, axis, up)
        after = lax.ppermute(first, axis, down)
        shard = jnp.concatenate([before, shard, after], axis=dim)
    return shard


def grouped_view(values):
    return values.reshape(
        values.shape[0], values.shape[1] * values.shape[2], GROUPS, values.shape[3] // GROUPS
    )


def group_sums(values):
    per = jnp.sum(values, axis=(1, 2))
    return jnp.sum(per.reshape(per.shape[0], GROUPS, per.shape[1] // GROUPS), axis=2)


def per_channel(stats, channels):
    wide = jnp.repeat(stats, channels // GROUPS, axis=1)
    return wide[:, None, None, :]


def widen_columns(values):
    return jnp.pad(values, ((0, 0), (0, 0), (1, 1), (0, 0)))


def plane_windows(plane, rows_here, columns, flip):
    taps = []
    for row_tap in range(3):
        for col_tap in range(3):
            r0 = 2 - row_tap if flip else row_tap
            c0 = 2 - col_tap if flip else col_tap
            window = plane[r0 : r0 + rows_here, c0 : c0 + columns]
            taps.append(window.reshape(rows_here * columns, 1, plane.shape[-1]))
    return jnp.concatenate(taps, axis=1)


def shards(latent, norm_gain, conv_weight, grad_out):
    frames_here, rows_here, columns, channels = latent.shape
    cell_count = lax.axis_size("rows") * rows_here * columns * (channels // GROUPS)
    full_weight = lax.all_gather(conv_weight, "tm", axis=1, tiled=True)
    after_one = shifted(grad_out, "tm", -1)
    after_two = shifted(grad_out, "tm", -2)
    padded_grad = with_halo(
        jnp.concatenate([grad_out, after_one, after_two], axis=0), (("rows", 1),), 1
    )
    padded_grad = widen_columns(padded_grad)
    latent_block = jnp.concatenate(
        [shifted(latent, "tm", 2), shifted(latent, "tm", 1), latent], axis=0
    )
    latent_padded = with_halo(latent_block, (("rows", 1),), 1)
    latent_wide = latent.astype(jnp.float32)
    block_wide = latent_block.astype(jnp.float32)
    average_block = lax.psum(group_sums(block_wide), "rows") / cell_count
    centred_block = block_wide - per_channel(average_block, channels)
    spread_block = lax.psum(group_sums(centred_block * centred_block), "rows") / cell_count
    inverse_block = lax.rsqrt(spread_block + epsilon)
    inverse = per_channel(inverse_block[2:], channels)
    normed = centred_block[2:] * inverse
    scaled = normed * norm_gain
    sigmoid_value = jax.nn.sigmoid(scaled)
    padded_average = per_channel(average_block, channels)
    padded_inverse = per_channel(inverse_block, channels)
    normed_padded = (latent_padded.astype(jnp.float32) - padded_average) * padded_inverse
    scaled_padded = normed_padded * norm_gain
    activated_padded = (scaled_padded * jax.nn.sigmoid(scaled_padded)).astype(jnp.bfloat16)
    frame_index = lax.axis_index("tm") * frames_here - 2 + lax.iota(jnp.int32, 3)
    row_index = lax.axis_index("rows") * rows_here - 1 + lax.iota(jnp.int32, rows_here + 2)
    inside = (frame_index[:, None] >= 0) & (row_index[None, :] >= 0)
    inside = inside & (row_index[None, :] < lax.axis_size("rows") * rows_here)
    padded = jnp.where(inside[:, :, None, None], activated_padded, jnp.zeros_like(activated_padded))
    padded = widen_columns(padded)
    positions = frames_here * rows_here * columns
    full_weight, padded, padded_grad = lax.optimization_barrier((full_weight, padded, padded_grad))
    grad_act = None
    for time_tap in range(3):
        part = full_weight[9 * time_tap : 9 * time_tap + 9]
        back = plane_windows(padded_grad[2 - time_tap], rows_here, columns, True)
        term = lax.dot_general(
            back, part, (((1, 2), (0, 2)), ((), ())), preferred_element_type=jnp.float32
        )
        grad_act = term if grad_act is None else grad_act + term
    grad_scaled = (
        grad_act.reshape(latent.shape) * sigmoid_value * (1.0 + scaled * (1.0 - sigmoid_value))
    )
    grad_normed = grad_scaled * norm_gain
    partial = jnp.stack([group_sums(grad_normed), group_sums(grad_normed * normed)])
    full_weight, padded, partial = lax.optimization_barrier((full_weight, padded, partial))
    size = lax.axis_size("rows")
    steps = []
    step = 1
    while step < size:
        steps.append(step)
        step *= 2
    total = partial
    conv_sum = None
    for time_tap in range(max(3, len(steps))):
        if time_tap < len(steps):
            route = [(i, i ^ steps[time_tap]) for i in range(size)]
            total = total + lax.ppermute(total, "rows", route)
        if time_tap < 3:
            part = full_weight[9 * time_tap : 9 * time_tap + 9]
            fwd = plane_windows(padded[time_tap], rows_here, columns, False)
            term = jnp.dot(
                fwd.reshape(positions, 9 * channels),
                part.reshape(9 * channels, channels),
                preferred_element_type=jnp.float32,
            )
            conv_sum = term if conv_sum is None else conv_sum + term
        total, conv_sum, padded = lax.optimization_barrier((total, conv_sum, padded))
    first_sum, second_sum = total
    refined = (latent_wide + conv_sum.reshape(latent.shape)).astype(jnp.bfloat16)
    first = first_sum / cell_count
    second = second_sum / cell_count
    first_wide = per_channel(first, channels)
    second_wide = per_channel(second, channels)
    grad_norm_part = (grad_normed - first_wide - normed * second_wide) * inverse
    grad_latent = grad_out.astype(jnp.float32) + grad_norm_part
    return (refined, grad_latent)


def solution(mesh):
    placed = (P("tm", "rows", None, None), P(), P(None, "tm", None), P("tm", "rows", None, None))
    return jax.shard_map(
        shards,
        mesh=mesh,
        in_specs=placed,
        out_specs=(P("tm", "rows", None, None), P("tm", "rows", None, None)),
        check_vma=False,
    )
```

```python
import jax
import jax.numpy as jnp
from jax import lax
from jax.sharding import PartitionSpec as P

GROUPS = 32


epsilon = 1e-06


def shifted(block, axis, distance):
    devices = range(lax.axis_size(axis))
    route = [(i - distance, i) for i in devices if i - distance in devices]
    return lax.ppermute(block, axis, route)


def with_halo(shard, sides, width):
    for axis, dim in sides:
        size, length = (lax.axis_size(axis), shard.shape[dim])
        up = [(i, (i + 1) % size) for i in range(size - 1)]
        down = [(j, i) for i, j in up]
        last = lax.slice_in_dim(shard, length - width, length, axis=dim)
        first = lax.slice_in_dim(shard, 0, width, axis=dim)
        before = lax.ppermute(last, axis, up)
        after = lax.ppermute(first, axis, down)
        shard = jnp.concatenate([before, shard, after], axis=dim)
    return shard


def grouped_view(values):
    return values.reshape(
        values.shape[0], values.shape[1] * values.shape[2], GROUPS, values.shape[3] // GROUPS
    )


def group_sums(values):
    per = jnp.sum(values, axis=(1, 2))
    return jnp.sum(per.reshape(per.shape[0], GROUPS, per.shape[1] // GROUPS), axis=2)


def per_channel(stats, channels):
    wide = jnp.repeat(stats, channels // GROUPS, axis=1)
    return wide[:, None, None, :]


def widen_columns(values):
    return jnp.pad(values, ((0, 0), (0, 0), (1, 1), (0, 0)))


def plane_windows(plane, rows_here, columns, flip):
    taps = []
    for row_tap in range(3):
        for col_tap in range(3):
            r0 = 2 - row_tap if flip else row_tap
            c0 = 2 - col_tap if flip else col_tap
            window = plane[r0 : r0 + rows_here, c0 : c0 + columns]
            taps.append(window.reshape(rows_here * columns, 1, plane.shape[-1]))
    return jnp.concatenate(taps, axis=1)


def shards(latent, norm_gain, conv_weight, grad_out):
    frames_here, rows_here, columns, channels = latent.shape
    cell_count = lax.axis_size("rows") * rows_here * columns * (channels // GROUPS)
    full_weight = lax.all_gather(conv_weight, "tm", axis=1, tiled=True)
    after_one = shifted(grad_out, "tm", -1)
    after_two = shifted(grad_out, "tm", -2)
    padded_grad = with_halo(
        jnp.concatenate([grad_out, after_one, after_two], axis=0), (("rows", 1),), 1
    )
    padded_grad = widen_columns(padded_grad)
    latent_block = jnp.concatenate(
        [shifted(latent, "tm", 2), shifted(latent, "tm", 1), latent], axis=0
    )
    latent_padded = with_halo(latent_block, (("rows", 1),), 1)
    latent_wide = latent.astype(jnp.float32)
    block_wide = latent_block.astype(jnp.float32)
    padded_grad, block_wide = lax.optimization_barrier((padded_grad, block_wide))
    average_block = lax.psum(group_sums(block_wide), "rows") / cell_count
    centred_block = block_wide - per_channel(average_block, channels)
    spread_block = lax.psum(group_sums(centred_block * centred_block), "rows") / cell_count
    inverse_block = lax.rsqrt(spread_block + epsilon)
    inverse = per_channel(inverse_block[2:], channels)
    normed = centred_block[2:] * inverse
    scaled = normed * norm_gain
    sigmoid_value = jax.nn.sigmoid(scaled)
    padded_average = per_channel(average_block, channels)
    padded_inverse = per_channel(inverse_block, channels)
    normed_padded = (latent_padded.astype(jnp.float32) - padded_average) * padded_inverse
    scaled_padded = normed_padded * norm_gain
    activated_padded = (scaled_padded * jax.nn.sigmoid(scaled_padded)).astype(jnp.bfloat16)
    frame_index = lax.axis_index("tm") * frames_here - 2 + lax.iota(jnp.int32, 3)
    row_index = lax.axis_index("rows") * rows_here - 1 + lax.iota(jnp.int32, rows_here + 2)
    inside = (frame_index[:, None] >= 0) & (row_index[None, :] >= 0)
    inside = inside & (row_index[None, :] < lax.axis_size("rows") * rows_here)
    padded = jnp.where(inside[:, :, None, None], activated_padded, jnp.zeros_like(activated_padded))
    padded = widen_columns(padded)
    positions = frames_here * rows_here * columns
    full_weight, padded, padded_grad = lax.optimization_barrier((full_weight, padded, padded_grad))
    grad_act = None
    for time_tap in range(3):
        part = full_weight[9 * time_tap : 9 * time_tap + 9]
        back = plane_windows(padded_grad[2 - time_tap], rows_here, columns, True)
        term = lax.dot_general(
            back, part, (((1, 2), (0, 2)), ((), ())), preferred_element_type=jnp.float32
        )
        grad_act = term if grad_act is None else grad_act + term
    grad_scaled = (
        grad_act.reshape(latent.shape) * sigmoid_value * (1.0 + scaled * (1.0 - sigmoid_value))
    )
    grad_normed = grad_scaled * norm_gain
    partial = jnp.stack([group_sums(grad_normed), group_sums(grad_normed * normed)])
    full_weight, padded, partial = lax.optimization_barrier((full_weight, padded, partial))
    size = lax.axis_size("rows")
    steps = []
    step = 1
    while step < size:
        steps.append(step)
        step *= 2
    total = partial
    conv_sum = None
    for time_tap in range(max(3, len(steps))):
        if time_tap < len(steps):
            route = [(i, i ^ steps[time_tap]) for i in range(size)]
            total = total + lax.ppermute(total, "rows", route)
        if time_tap < 3:
            part = full_weight[9 * time_tap : 9 * time_tap + 9]
            fwd = plane_windows(padded[time_tap], rows_here, columns, False)
            term = jnp.dot(
                fwd.reshape(positions, 9 * channels),
                part.reshape(9 * channels, channels),
                preferred_element_type=jnp.float32,
            )
            conv_sum = term if conv_sum is None else conv_sum + term
        total, conv_sum, padded = lax.optimization_barrier((total, conv_sum, padded))
    first_sum, second_sum = total
    refined = (latent_wide + conv_sum.reshape(latent.shape)).astype(jnp.bfloat16)
    first = first_sum / cell_count
    second = second_sum / cell_count
    first_wide = per_channel(first, channels)
    second_wide = per_channel(second, channels)
    grad_norm_part = (grad_normed - first_wide - normed * second_wide) * inverse
    grad_latent = grad_out.astype(jnp.float32) + grad_norm_part
    return (refined, grad_latent)


def solution(mesh):
    placed = (P("tm", "rows", None, None), P(), P(None, "tm", None), P("tm", "rows", None, None))
    return jax.shard_map(
        shards,
        mesh=mesh,
        in_specs=placed,
        out_specs=(P("tm", "rows", None, None), P("tm", "rows", None, None)),
        check_vma=False,
    )
```

```python
import jax
import jax.numpy as jnp
from jax import lax
from jax.sharding import PartitionSpec as P

GROUPS = 32


epsilon = 1e-06


def shifted(block, axis, distance):
    devices = range(lax.axis_size(axis))
    route = [(i - distance, i) for i in devices if i - distance in devices]
    return lax.ppermute(block, axis, route)


def with_halo(shard, sides, width):
    for axis, dim in sides:
        size, length = (lax.axis_size(axis), shard.shape[dim])
        up = [(i, (i + 1) % size) for i in range(size - 1)]
        down = [(j, i) for i, j in up]
        last = lax.slice_in_dim(shard, length - width, length, axis=dim)
        first = lax.slice_in_dim(shard, 0, width, axis=dim)
        before = lax.ppermute(last, axis, up)
        after = lax.ppermute(first, axis, down)
        shard = jnp.concatenate([before, shard, after], axis=dim)
    return shard


def grouped_view(values):
    return values.reshape(
        values.shape[0], values.shape[1] * values.shape[2], GROUPS, values.shape[3] // GROUPS
    )


def group_sums(values):
    per = jnp.sum(values, axis=(1, 2))
    return jnp.sum(per.reshape(per.shape[0], GROUPS, per.shape[1] // GROUPS), axis=2)


def per_channel(stats, channels):
    wide = jnp.repeat(stats, channels // GROUPS, axis=1)
    return wide[:, None, None, :]


def widen_columns(values):
    return jnp.pad(values, ((0, 0), (0, 0), (1, 1), (0, 0)))


def plane_windows(plane, rows_here, columns, flip):
    taps = []
    for row_tap in range(3):
        for col_tap in range(3):
            r0 = 2 - row_tap if flip else row_tap
            c0 = 2 - col_tap if flip else col_tap
            window = plane[r0 : r0 + rows_here, c0 : c0 + columns]
            taps.append(window.reshape(rows_here * columns, 1, plane.shape[-1]))
    return jnp.concatenate(taps, axis=1)


def shards(latent, norm_gain, conv_weight, grad_out):
    frames_here, rows_here, columns, channels = latent.shape
    cell_count = lax.axis_size("rows") * rows_here * columns * (channels // GROUPS)
    full_weight = lax.all_gather(conv_weight, "tm", axis=1, tiled=True)
    after_one = shifted(grad_out, "tm", -1)
    after_two = shifted(grad_out, "tm", -2)
    padded_grad = with_halo(
        jnp.concatenate([grad_out, after_one, after_two], axis=0), (("rows", 1),), 1
    )
    padded_grad = widen_columns(padded_grad)
    latent_block = jnp.concatenate(
        [shifted(latent, "tm", 2), shifted(latent, "tm", 1), latent], axis=0
    )
    latent_padded = with_halo(latent_block, (("rows", 1),), 1)
    latent_wide = latent.astype(jnp.float32)
    block_wide = latent_block.astype(jnp.float32)
    local_count = rows_here * columns * (channels // GROUPS)
    local_sum = group_sums(block_wide)
    local_centred = block_wide - per_channel(local_sum / local_count, channels)
    local_square = group_sums(local_centred * local_centred)
    gathered = lax.all_gather(jnp.stack([local_sum, local_square]), "rows", axis=0)
    average_block = jnp.sum(gathered[:, 0], axis=0) / cell_count
    offset = gathered[:, 0] / local_count - average_block
    square_total = jnp.sum(gathered[:, 1], axis=0) + local_count * jnp.sum(offset * offset, axis=0)
    spread_block = square_total / cell_count
    centred_block = block_wide - per_channel(average_block, channels)
    inverse_block = lax.rsqrt(spread_block + epsilon)
    inverse = per_channel(inverse_block[2:], channels)
    normed = centred_block[2:] * inverse
    scaled = normed * norm_gain
    sigmoid_value = jax.nn.sigmoid(scaled)
    padded_average = per_channel(average_block, channels)
    padded_inverse = per_channel(inverse_block, channels)
    normed_padded = (latent_padded.astype(jnp.float32) - padded_average) * padded_inverse
    scaled_padded = normed_padded * norm_gain
    activated_padded = (scaled_padded * jax.nn.sigmoid(scaled_padded)).astype(jnp.bfloat16)
    frame_index = lax.axis_index("tm") * frames_here - 2 + lax.iota(jnp.int32, 3)
    row_index = lax.axis_index("rows") * rows_here - 1 + lax.iota(jnp.int32, rows_here + 2)
    inside = (frame_index[:, None] >= 0) & (row_index[None, :] >= 0)
    inside = inside & (row_index[None, :] < lax.axis_size("rows") * rows_here)
    padded = jnp.where(inside[:, :, None, None], activated_padded, jnp.zeros_like(activated_padded))
    padded = widen_columns(padded)
    positions = frames_here * rows_here * columns
    full_weight, padded, padded_grad = lax.optimization_barrier((full_weight, padded, padded_grad))
    grad_act = None
    for time_tap in range(3):
        part = full_weight[9 * time_tap : 9 * time_tap + 9]
        back = plane_windows(padded_grad[2 - time_tap], rows_here, columns, True)
        term = lax.dot_general(
            back, part, (((1, 2), (0, 2)), ((), ())), preferred_element_type=jnp.float32
        )
        grad_act = term if grad_act is None else grad_act + term
    grad_scaled = (
        grad_act.reshape(latent.shape) * sigmoid_value * (1.0 + scaled * (1.0 - sigmoid_value))
    )
    grad_normed = grad_scaled * norm_gain
    partial = jnp.stack([group_sums(grad_normed), group_sums(grad_normed * normed)])
    full_weight, padded, partial = lax.optimization_barrier((full_weight, padded, partial))
    size = lax.axis_size("rows")
    steps = []
    step = 1
    while step < size:
        steps.append(step)
        step *= 2
    total = partial
    conv_sum = None
    for time_tap in range(max(3, len(steps))):
        if time_tap < len(steps):
            route = [(i, i ^ steps[time_tap]) for i in range(size)]
            total = total + lax.ppermute(total, "rows", route)
        if time_tap < 3:
            part = full_weight[9 * time_tap : 9 * time_tap + 9]
            fwd = plane_windows(padded[time_tap], rows_here, columns, False)
            term = jnp.dot(
                fwd.reshape(positions, 9 * channels),
                part.reshape(9 * channels, channels),
                preferred_element_type=jnp.float32,
            )
            conv_sum = term if conv_sum is None else conv_sum + term
        total, conv_sum, padded = lax.optimization_barrier((total, conv_sum, padded))
    first_sum, second_sum = total
    refined = (latent_wide + conv_sum.reshape(latent.shape)).astype(jnp.bfloat16)
    first = first_sum / cell_count
    second = second_sum / cell_count
    first_wide = per_channel(first, channels)
    second_wide = per_channel(second, channels)
    grad_norm_part = (grad_normed - first_wide - normed * second_wide) * inverse
    grad_latent = grad_out.astype(jnp.float32) + grad_norm_part
    return (refined, grad_latent)


def solution(mesh):
    placed = (P("tm", "rows", None, None), P(), P(None, "tm", None), P("tm", "rows", None, None))
    return jax.shard_map(
        shards,
        mesh=mesh,
        in_specs=placed,
        out_specs=(P("tm", "rows", None, None), P("tm", "rows", None, None)),
        check_vma=False,
    )
```

```python
import jax
import jax.numpy as jnp
from jax import lax
from jax.sharding import PartitionSpec as P

GROUPS = 32


epsilon = 1e-06


def shifted(block, axis, distance):
    devices = range(lax.axis_size(axis))
    route = [(i - distance, i) for i in devices if i - distance in devices]
    return lax.ppermute(block, axis, route)


def with_halo(shard, sides, width):
    for axis, dim in sides:
        size, length = (lax.axis_size(axis), shard.shape[dim])
        up = [(i, (i + 1) % size) for i in range(size - 1)]
        down = [(j, i) for i, j in up]
        last = lax.slice_in_dim(shard, length - width, length, axis=dim)
        first = lax.slice_in_dim(shard, 0, width, axis=dim)
        before = lax.ppermute(last, axis, up)
        after = lax.ppermute(first, axis, down)
        shard = jnp.concatenate([before, shard, after], axis=dim)
    return shard


def grouped_view(values):
    return values.reshape(
        values.shape[0], values.shape[1] * values.shape[2], GROUPS, values.shape[3] // GROUPS
    )


def group_sums(values):
    per = jnp.sum(values, axis=(1, 2))
    return jnp.sum(per.reshape(per.shape[0], GROUPS, per.shape[1] // GROUPS), axis=2)


def per_channel(stats, channels):
    wide = jnp.repeat(stats, channels // GROUPS, axis=1)
    return wide[:, None, None, :]


def widen_columns(values):
    return jnp.pad(values, ((0, 0), (0, 0), (1, 1), (0, 0)))


def plane_windows(plane, rows_here, columns, flip):
    taps = []
    for row_tap in range(3):
        for col_tap in range(3):
            r0 = 2 - row_tap if flip else row_tap
            c0 = 2 - col_tap if flip else col_tap
            window = plane[r0 : r0 + rows_here, c0 : c0 + columns]
            taps.append(window.reshape(rows_here * columns, 1, plane.shape[-1]))
    return jnp.concatenate(taps, axis=1)


def shards(latent, norm_gain, conv_weight, grad_out):
    frames_here, rows_here, columns, channels = latent.shape
    cell_count = lax.axis_size("rows") * rows_here * columns * (channels // GROUPS)
    full_weight = lax.all_gather(conv_weight, "tm", axis=1, tiled=True)
    grad_rows = with_halo(grad_out, (("rows", 1),), 1)
    padded_grad = jnp.concatenate(
        [grad_rows, shifted(grad_rows, "tm", -1), shifted(grad_rows, "tm", -2)], axis=0
    )
    padded_grad = widen_columns(padded_grad)
    latent_rows = with_halo(latent, (("rows", 1),), 1)
    latent_padded = jnp.concatenate(
        [shifted(latent_rows, "tm", 2), shifted(latent_rows, "tm", 1), latent_rows], axis=0
    )
    latent_block = latent_padded[:, 1 : 1 + rows_here]
    latent_wide = latent.astype(jnp.float32)
    block_wide = latent_block.astype(jnp.float32)
    local_count = rows_here * columns * (channels // GROUPS)
    local_sum = group_sums(block_wide)
    local_centred = block_wide - per_channel(local_sum / local_count, channels)
    local_square = group_sums(local_centred * local_centred)
    gathered = lax.all_gather(jnp.stack([local_sum, local_square]), "rows", axis=0)
    average_block = jnp.sum(gathered[:, 0], axis=0) / cell_count
    offset = gathered[:, 0] / local_count - average_block
    square_total = jnp.sum(gathered[:, 1], axis=0) + local_count * jnp.sum(offset * offset, axis=0)
    spread_block = square_total / cell_count
    centred_block = block_wide - per_channel(average_block, channels)
    inverse_block = lax.rsqrt(spread_block + epsilon)
    inverse = per_channel(inverse_block[2:], channels)
    normed = centred_block[2:] * inverse
    scaled = normed * norm_gain
    sigmoid_value = jax.nn.sigmoid(scaled)
    padded_average = per_channel(average_block, channels)
    padded_inverse = per_channel(inverse_block, channels)
    normed_padded = (latent_padded.astype(jnp.float32) - padded_average) * padded_inverse
    scaled_padded = normed_padded * norm_gain
    activated_padded = (scaled_padded * jax.nn.sigmoid(scaled_padded)).astype(jnp.bfloat16)
    frame_index = lax.axis_index("tm") * frames_here - 2 + lax.iota(jnp.int32, 3)
    row_index = lax.axis_index("rows") * rows_here - 1 + lax.iota(jnp.int32, rows_here + 2)
    inside = (frame_index[:, None] >= 0) & (row_index[None, :] >= 0)
    inside = inside & (row_index[None, :] < lax.axis_size("rows") * rows_here)
    padded = jnp.where(inside[:, :, None, None], activated_padded, jnp.zeros_like(activated_padded))
    padded = widen_columns(padded)
    positions = frames_here * rows_here * columns
    full_weight, padded, padded_grad = lax.optimization_barrier((full_weight, padded, padded_grad))
    grad_act = None
    for time_tap in range(3):
        part = full_weight[9 * time_tap : 9 * time_tap + 9]
        back = plane_windows(padded_grad[2 - time_tap], rows_here, columns, True)
        term = lax.dot_general(
            back, part, (((1, 2), (0, 2)), ((), ())), preferred_element_type=jnp.float32
        )
        grad_act = term if grad_act is None else grad_act + term
    grad_scaled = (
        grad_act.reshape(latent.shape) * sigmoid_value * (1.0 + scaled * (1.0 - sigmoid_value))
    )
    grad_normed = grad_scaled * norm_gain
    partial = jnp.stack([group_sums(grad_normed), group_sums(grad_normed * normed)])
    full_weight, padded, partial = lax.optimization_barrier((full_weight, padded, partial))
    size = lax.axis_size("rows")
    steps = []
    step = 1
    while step < size:
        steps.append(step)
        step *= 2
    total = partial
    conv_sum = None
    for time_tap in range(max(3, len(steps))):
        if time_tap < len(steps):
            route = [(i, i ^ steps[time_tap]) for i in range(size)]
            total = total + lax.ppermute(total, "rows", route)
        if time_tap < 3:
            part = full_weight[9 * time_tap : 9 * time_tap + 9]
            fwd = plane_windows(padded[time_tap], rows_here, columns, False)
            term = jnp.dot(
                fwd.reshape(positions, 9 * channels),
                part.reshape(9 * channels, channels),
                preferred_element_type=jnp.float32,
            )
            conv_sum = term if conv_sum is None else conv_sum + term
        total, conv_sum, padded = lax.optimization_barrier((total, conv_sum, padded))
    first_sum, second_sum = total
    refined = (latent_wide + conv_sum.reshape(latent.shape)).astype(jnp.bfloat16)
    first = first_sum / cell_count
    second = second_sum / cell_count
    first_wide = per_channel(first, channels)
    second_wide = per_channel(second, channels)
    grad_norm_part = (grad_normed - first_wide - normed * second_wide) * inverse
    grad_latent = grad_out.astype(jnp.float32) + grad_norm_part
    return (refined, grad_latent)


def solution(mesh):
    placed = (P("tm", "rows", None, None), P(), P(None, "tm", None), P("tm", "rows", None, None))
    return jax.shard_map(
        shards,
        mesh=mesh,
        in_specs=placed,
        out_specs=(P("tm", "rows", None, None), P("tm", "rows", None, None)),
        check_vma=False,
    )
```

```python
import jax
import jax.numpy as jnp
from jax import lax
from jax.sharding import PartitionSpec as P

GROUPS = 32


epsilon = 1e-06


def shifted(block, axis, distance):
    devices = range(lax.axis_size(axis))
    route = [(i - distance, i) for i in devices if i - distance in devices]
    return lax.ppermute(block, axis, route)


def with_halo(shard, sides, width):
    for axis, dim in sides:
        size, length = (lax.axis_size(axis), shard.shape[dim])
        up = [(i, (i + 1) % size) for i in range(size - 1)]
        down = [(j, i) for i, j in up]
        last = lax.slice_in_dim(shard, length - width, length, axis=dim)
        first = lax.slice_in_dim(shard, 0, width, axis=dim)
        before = lax.ppermute(last, axis, up)
        after = lax.ppermute(first, axis, down)
        shard = jnp.concatenate([before, shard, after], axis=dim)
    return shard


def grouped_view(values):
    return values.reshape(
        values.shape[0], values.shape[1] * values.shape[2], GROUPS, values.shape[3] // GROUPS
    )


def group_sums(values):
    per = jnp.sum(values, axis=(1, 2))
    return jnp.sum(per.reshape(per.shape[0], GROUPS, per.shape[1] // GROUPS), axis=2)


def per_channel(stats, channels):
    wide = jnp.repeat(stats, channels // GROUPS, axis=1)
    return wide[:, None, None, :]


def widen_columns(values):
    return jnp.pad(values, ((0, 0), (0, 0), (1, 1), (0, 0)))


def plane_windows(plane, rows_here, columns, flip):
    taps = []
    for row_tap in range(3):
        for col_tap in range(3):
            r0 = 2 - row_tap if flip else row_tap
            c0 = 2 - col_tap if flip else col_tap
            window = plane[r0 : r0 + rows_here, c0 : c0 + columns]
            taps.append(window.reshape(rows_here * columns, 1, plane.shape[-1]))
    return jnp.concatenate(taps, axis=1)


def shards(latent, norm_gain, conv_weight, grad_out):
    frames_here, rows_here, columns, channels = latent.shape
    cell_count = lax.axis_size("rows") * rows_here * columns * (channels // GROUPS)
    full_weight = lax.all_gather(conv_weight, "tm", axis=1, tiled=True)
    latent_block = jnp.concatenate(
        [shifted(latent, "tm", 2), shifted(latent, "tm", 1), latent], axis=0
    )
    latent_padded = with_halo(latent_block, (("rows", 1),), 1)
    latent_wide = latent.astype(jnp.float32)
    block_wide = latent_block.astype(jnp.float32)
    average_block = lax.psum(group_sums(block_wide), "rows") / cell_count
    centred_block = block_wide - per_channel(average_block, channels)
    spread_block = lax.psum(group_sums(centred_block * centred_block), "rows") / cell_count
    inverse_block = lax.rsqrt(spread_block + epsilon)
    grad_source, inverse_block = lax.optimization_barrier((grad_out, inverse_block))
    after_one = shifted(grad_source, "tm", -1)
    after_two = shifted(grad_source, "tm", -2)
    padded_grad = with_halo(
        jnp.concatenate([grad_source, after_one, after_two], axis=0), (("rows", 1),), 1
    )
    padded_grad = widen_columns(padded_grad)
    inverse = per_channel(inverse_block[2:], channels)
    normed = centred_block[2:] * inverse
    scaled = normed * norm_gain
    sigmoid_value = jax.nn.sigmoid(scaled)
    padded_average = per_channel(average_block, channels)
    padded_inverse = per_channel(inverse_block, channels)
    normed_padded = (latent_padded.astype(jnp.float32) - padded_average) * padded_inverse
    scaled_padded = normed_padded * norm_gain
    activated_padded = (scaled_padded * jax.nn.sigmoid(scaled_padded)).astype(jnp.bfloat16)
    frame_index = lax.axis_index("tm") * frames_here - 2 + lax.iota(jnp.int32, 3)
    row_index = lax.axis_index("rows") * rows_here - 1 + lax.iota(jnp.int32, rows_here + 2)
    inside = (frame_index[:, None] >= 0) & (row_index[None, :] >= 0)
    inside = inside & (row_index[None, :] < lax.axis_size("rows") * rows_here)
    padded = jnp.where(inside[:, :, None, None], activated_padded, jnp.zeros_like(activated_padded))
    padded = widen_columns(padded)
    positions = frames_here * rows_here * columns
    full_weight, padded, padded_grad = lax.optimization_barrier((full_weight, padded, padded_grad))
    grad_act = None
    for time_tap in range(3):
        part = full_weight[9 * time_tap : 9 * time_tap + 9]
        back = plane_windows(padded_grad[2 - time_tap], rows_here, columns, True)
        term = lax.dot_general(
            back, part, (((1, 2), (0, 2)), ((), ())), preferred_element_type=jnp.float32
        )
        grad_act = term if grad_act is None else grad_act + term
    grad_scaled = (
        grad_act.reshape(latent.shape) * sigmoid_value * (1.0 + scaled * (1.0 - sigmoid_value))
    )
    grad_normed = grad_scaled * norm_gain
    partial = jnp.stack([group_sums(grad_normed), group_sums(grad_normed * normed)])
    full_weight, padded, partial = lax.optimization_barrier((full_weight, padded, partial))
    size = lax.axis_size("rows")
    steps = []
    step = 1
    while step < size:
        steps.append(step)
        step *= 2
    total = partial
    conv_sum = None
    for time_tap in range(max(3, len(steps))):
        if time_tap < len(steps):
            route = [(i, i ^ steps[time_tap]) for i in range(size)]
            total = total + lax.ppermute(total, "rows", route)
        if time_tap < 3:
            part = full_weight[9 * time_tap : 9 * time_tap + 9]
            fwd = plane_windows(padded[time_tap], rows_here, columns, False)
            term = jnp.dot(
                fwd.reshape(positions, 9 * channels),
                part.reshape(9 * channels, channels),
                preferred_element_type=jnp.float32,
            )
            conv_sum = term if conv_sum is None else conv_sum + term
        total, conv_sum, padded = lax.optimization_barrier((total, conv_sum, padded))
    first_sum, second_sum = total
    refined = (latent_wide + conv_sum.reshape(latent.shape)).astype(jnp.bfloat16)
    first = first_sum / cell_count
    second = second_sum / cell_count
    first_wide = per_channel(first, channels)
    second_wide = per_channel(second, channels)
    grad_norm_part = (grad_normed - first_wide - normed * second_wide) * inverse
    grad_latent = grad_out.astype(jnp.float32) + grad_norm_part
    return (refined, grad_latent)


def solution(mesh):
    placed = (P("tm", "rows", None, None), P(), P(None, "tm", None), P("tm", "rows", None, None))
    return jax.shard_map(
        shards,
        mesh=mesh,
        in_specs=placed,
        out_specs=(P("tm", "rows", None, None), P("tm", "rows", None, None)),
        check_vma=False,
    )
```

```python
import jax
import jax.numpy as jnp
from jax import lax
from jax.sharding import PartitionSpec as P

GROUPS = 32


epsilon = 1e-06


def shifted(block, axis, distance):
    devices = range(lax.axis_size(axis))
    route = [(i - distance, i) for i in devices if i - distance in devices]
    return lax.ppermute(block, axis, route)


def with_halo(shard, sides, width):
    for axis, dim in sides:
        size, length = (lax.axis_size(axis), shard.shape[dim])
        up = [(i, (i + 1) % size) for i in range(size - 1)]
        down = [(j, i) for i, j in up]
        last = lax.slice_in_dim(shard, length - width, length, axis=dim)
        first = lax.slice_in_dim(shard, 0, width, axis=dim)
        before = lax.ppermute(last, axis, up)
        after = lax.ppermute(first, axis, down)
        shard = jnp.concatenate([before, shard, after], axis=dim)
    return shard


def grouped_view(values):
    return values.reshape(
        values.shape[0], values.shape[1] * values.shape[2], GROUPS, values.shape[3] // GROUPS
    )


def group_sums(values):
    per = jnp.sum(values, axis=(1, 2))
    return jnp.sum(per.reshape(per.shape[0], GROUPS, per.shape[1] // GROUPS), axis=2)


def per_channel(stats, channels):
    wide = jnp.repeat(stats, channels // GROUPS, axis=1)
    return wide[:, None, None, :]


def widen_columns(values):
    return jnp.pad(values, ((0, 0), (0, 0), (1, 1), (0, 0)))


def plane_windows(plane, rows_here, columns, flip):
    taps = []
    for row_tap in range(3):
        for col_tap in range(3):
            r0 = 2 - row_tap if flip else row_tap
            c0 = 2 - col_tap if flip else col_tap
            window = plane[r0 : r0 + rows_here, c0 : c0 + columns]
            taps.append(window.reshape(rows_here * columns, 1, plane.shape[-1]))
    return jnp.concatenate(taps, axis=1)


def shards(latent, norm_gain, conv_weight, grad_out):
    frames_here, rows_here, columns, channels = latent.shape
    cell_count = lax.axis_size("rows") * rows_here * columns * (channels // GROUPS)
    full_weight = lax.all_gather(conv_weight, "tm", axis=1, tiled=True)
    after_one = shifted(grad_out, "tm", -1)
    after_two = shifted(grad_out, "tm", -2)
    padded_grad = with_halo(
        jnp.concatenate([grad_out, after_one, after_two], axis=0), (("rows", 1),), 1
    )
    padded_grad = widen_columns(padded_grad)
    latent_block = jnp.concatenate(
        [shifted(latent, "tm", 2), shifted(latent, "tm", 1), latent], axis=0
    )
    latent_padded = with_halo(latent_block, (("rows", 1),), 1)
    latent_wide = latent.astype(jnp.float32)
    average = lax.psum(group_sums(latent_wide), "rows") / cell_count
    centred = latent_wide - per_channel(average, channels)
    spread = lax.psum(group_sums(centred * centred), "rows") / cell_count
    own_stats = jnp.concatenate([average, lax.rsqrt(spread + epsilon)], axis=0)
    stats_block = jnp.stack(
        [shifted(own_stats, "tm", 2), shifted(own_stats, "tm", 1), own_stats], axis=1
    )
    average_block, inverse_block = stats_block[0], stats_block[1]
    inverse = per_channel(own_stats[1:], channels)
    normed = centred * inverse
    scaled = normed * norm_gain
    sigmoid_value = jax.nn.sigmoid(scaled)
    padded_average = per_channel(average_block, channels)
    padded_inverse = per_channel(inverse_block, channels)
    normed_padded = (latent_padded.astype(jnp.float32) - padded_average) * padded_inverse
    scaled_padded = normed_padded * norm_gain
    activated_padded = (scaled_padded * jax.nn.sigmoid(scaled_padded)).astype(jnp.bfloat16)
    frame_index = lax.axis_index("tm") * frames_here - 2 + lax.iota(jnp.int32, 3)
    row_index = lax.axis_index("rows") * rows_here - 1 + lax.iota(jnp.int32, rows_here + 2)
    inside = (frame_index[:, None] >= 0) & (row_index[None, :] >= 0)
    inside = inside & (row_index[None, :] < lax.axis_size("rows") * rows_here)
    padded = jnp.where(inside[:, :, None, None], activated_padded, jnp.zeros_like(activated_padded))
    padded = widen_columns(padded)
    positions = frames_here * rows_here * columns
    full_weight, padded, padded_grad = lax.optimization_barrier((full_weight, padded, padded_grad))
    grad_act = None
    for time_tap in range(3):
        part = full_weight[9 * time_tap : 9 * time_tap + 9]
        back = plane_windows(padded_grad[2 - time_tap], rows_here, columns, True)
        term = lax.dot_general(
            back, part, (((1, 2), (0, 2)), ((), ())), preferred_element_type=jnp.float32
        )
        grad_act = term if grad_act is None else grad_act + term
    grad_scaled = (
        grad_act.reshape(latent.shape) * sigmoid_value * (1.0 + scaled * (1.0 - sigmoid_value))
    )
    grad_normed = grad_scaled * norm_gain
    partial = jnp.stack([group_sums(grad_normed), group_sums(grad_normed * normed)])
    full_weight, padded, partial = lax.optimization_barrier((full_weight, padded, partial))
    size = lax.axis_size("rows")
    steps = []
    step = 1
    while step < size:
        steps.append(step)
        step *= 2
    total = partial
    conv_sum = None
    for time_tap in range(max(3, len(steps))):
        if time_tap < len(steps):
            route = [(i, i ^ steps[time_tap]) for i in range(size)]
            total = total + lax.ppermute(total, "rows", route)
        if time_tap < 3:
            part = full_weight[9 * time_tap : 9 * time_tap + 9]
            fwd = plane_windows(padded[time_tap], rows_here, columns, False)
            term = jnp.dot(
                fwd.reshape(positions, 9 * channels),
                part.reshape(9 * channels, channels),
                preferred_element_type=jnp.float32,
            )
            conv_sum = term if conv_sum is None else conv_sum + term
        total, conv_sum, padded = lax.optimization_barrier((total, conv_sum, padded))
    first_sum, second_sum = total
    refined = (latent_wide + conv_sum.reshape(latent.shape)).astype(jnp.bfloat16)
    first = first_sum / cell_count
    second = second_sum / cell_count
    first_wide = per_channel(first, channels)
    second_wide = per_channel(second, channels)
    grad_norm_part = (grad_normed - first_wide - normed * second_wide) * inverse
    grad_latent = grad_out.astype(jnp.float32) + grad_norm_part
    return (refined, grad_latent)


def solution(mesh):
    placed = (P("tm", "rows", None, None), P(), P(None, "tm", None), P("tm", "rows", None, None))
    return jax.shard_map(
        shards,
        mesh=mesh,
        in_specs=placed,
        out_specs=(P("tm", "rows", None, None), P("tm", "rows", None, None)),
        check_vma=False,
    )
```

```python
import jax
import jax.numpy as jnp
from jax import lax
from jax.sharding import PartitionSpec as P

GROUPS = 32


epsilon = 1e-06


def shifted(block, axis, distance):
    devices = range(lax.axis_size(axis))
    route = [(i - distance, i) for i in devices if i - distance in devices]
    return lax.ppermute(block, axis, route)


def with_halo(shard, sides, width):
    for axis, dim in sides:
        size, length = (lax.axis_size(axis), shard.shape[dim])
        up = [(i, (i + 1) % size) for i in range(size - 1)]
        down = [(j, i) for i, j in up]
        last = lax.slice_in_dim(shard, length - width, length, axis=dim)
        first = lax.slice_in_dim(shard, 0, width, axis=dim)
        before = lax.ppermute(last, axis, up)
        after = lax.ppermute(first, axis, down)
        shard = jnp.concatenate([before, shard, after], axis=dim)
    return shard


def grouped_view(values):
    return values.reshape(
        values.shape[0], values.shape[1] * values.shape[2], GROUPS, values.shape[3] // GROUPS
    )


def group_sums(values):
    per = jnp.sum(values, axis=(1, 2))
    return jnp.sum(per.reshape(per.shape[0], GROUPS, per.shape[1] // GROUPS), axis=2)


def per_channel(stats, channels):
    wide = jnp.repeat(stats, channels // GROUPS, axis=1)
    return wide[:, None, None, :]


def widen_columns(values):
    return jnp.pad(values, ((0, 0), (0, 0), (1, 1), (0, 0)))


def plane_windows(plane, rows_here, columns, flip):
    taps = []
    for row_tap in range(3):
        for col_tap in range(3):
            r0 = 2 - row_tap if flip else row_tap
            c0 = 2 - col_tap if flip else col_tap
            window = plane[r0 : r0 + rows_here, c0 : c0 + columns]
            taps.append(window.reshape(rows_here * columns, 1, plane.shape[-1]))
    return jnp.concatenate(taps, axis=1)


def shards(latent, norm_gain, conv_weight, grad_out):
    frames_here, rows_here, columns, channels = latent.shape
    cell_count = lax.axis_size("rows") * rows_here * columns * (channels // GROUPS)
    full_weight = lax.all_gather(conv_weight, "tm", axis=1, tiled=True)
    after_one = shifted(grad_out, "tm", -1)
    after_two = shifted(grad_out, "tm", -2)
    padded_grad = with_halo(
        jnp.concatenate([grad_out, after_one, after_two], axis=0), (("rows", 1),), 1
    )
    padded_grad = widen_columns(padded_grad)
    latent_block = jnp.concatenate(
        [shifted(latent, "tm", 2), shifted(latent, "tm", 1), latent], axis=0
    )
    latent_padded = with_halo(latent_block, (("rows", 1),), 1)
    latent_wide = latent.astype(jnp.float32)
    block_wide = latent_block.astype(jnp.float32)
    average_block = lax.psum(group_sums(block_wide), "rows") / cell_count
    centred_block = block_wide - per_channel(average_block, channels)
    spread_block = lax.psum(group_sums(centred_block * centred_block), "rows") / cell_count
    inverse_block = lax.rsqrt(spread_block + epsilon)
    inverse = per_channel(inverse_block[2:], channels)
    normed = centred_block[2:] * inverse
    scaled = normed * norm_gain
    sigmoid_value = jax.nn.sigmoid(scaled)
    slope = sigmoid_value * (1.0 + scaled * (1.0 - sigmoid_value)) * norm_gain
    padded_average = per_channel(average_block, channels)
    padded_inverse = per_channel(inverse_block, channels)
    normed_padded = (latent_padded.astype(jnp.float32) - padded_average) * padded_inverse
    scaled_padded = normed_padded * norm_gain
    activated_padded = (scaled_padded * jax.nn.sigmoid(scaled_padded)).astype(jnp.bfloat16)
    frame_index = lax.axis_index("tm") * frames_here - 2 + lax.iota(jnp.int32, 3)
    row_index = lax.axis_index("rows") * rows_here - 1 + lax.iota(jnp.int32, rows_here + 2)
    inside = (frame_index[:, None] >= 0) & (row_index[None, :] >= 0)
    inside = inside & (row_index[None, :] < lax.axis_size("rows") * rows_here)
    padded = jnp.where(inside[:, :, None, None], activated_padded, jnp.zeros_like(activated_padded))
    padded = widen_columns(padded)
    positions = frames_here * rows_here * columns
    full_weight, padded, padded_grad, slope = lax.optimization_barrier(
        (full_weight, padded, padded_grad, slope)
    )
    grad_act = None
    for time_tap in range(3):
        part = full_weight[9 * time_tap : 9 * time_tap + 9]
        back = plane_windows(padded_grad[2 - time_tap], rows_here, columns, True)
        term = lax.dot_general(
            back, part, (((1, 2), (0, 2)), ((), ())), preferred_element_type=jnp.float32
        )
        grad_act = term if grad_act is None else grad_act + term
    grad_normed = grad_act.reshape(latent.shape) * slope
    partial = jnp.stack([group_sums(grad_normed), group_sums(grad_normed * normed)])
    full_weight, padded, partial = lax.optimization_barrier((full_weight, padded, partial))
    size = lax.axis_size("rows")
    steps = []
    step = 1
    while step < size:
        steps.append(step)
        step *= 2
    total = partial
    conv_sum = None
    for time_tap in range(max(3, len(steps))):
        if time_tap < len(steps):
            route = [(i, i ^ steps[time_tap]) for i in range(size)]
            total = total + lax.ppermute(total, "rows", route)
        if time_tap < 3:
            part = full_weight[9 * time_tap : 9 * time_tap + 9]
            fwd = plane_windows(padded[time_tap], rows_here, columns, False)
            term = jnp.dot(
                fwd.reshape(positions, 9 * channels),
                part.reshape(9 * channels, channels),
                preferred_element_type=jnp.float32,
            )
            conv_sum = term if conv_sum is None else conv_sum + term
        total, conv_sum, padded = lax.optimization_barrier((total, conv_sum, padded))
    first_sum, second_sum = total
    refined = (latent_wide + conv_sum.reshape(latent.shape)).astype(jnp.bfloat16)
    first = first_sum / cell_count
    second = second_sum / cell_count
    first_wide = per_channel(first, channels)
    second_wide = per_channel(second, channels)
    grad_norm_part = (grad_normed - first_wide - normed * second_wide) * inverse
    grad_latent = grad_out.astype(jnp.float32) + grad_norm_part
    return (refined, grad_latent)


def solution(mesh):
    placed = (P("tm", "rows", None, None), P(), P(None, "tm", None), P("tm", "rows", None, None))
    return jax.shard_map(
        shards,
        mesh=mesh,
        in_specs=placed,
        out_specs=(P("tm", "rows", None, None), P("tm", "rows", None, None)),
        check_vma=False,
    )
```

```python
import jax
import jax.numpy as jnp
from jax import lax
from jax.sharding import PartitionSpec as P

GROUPS = 32


epsilon = 1e-06


def shifted(block, axis, distance):
    devices = range(lax.axis_size(axis))
    route = [(i - distance, i) for i in devices if i - distance in devices]
    return lax.ppermute(block, axis, route)


def with_halo(shard, sides, width):
    for axis, dim in sides:
        size, length = (lax.axis_size(axis), shard.shape[dim])
        up = [(i, (i + 1) % size) for i in range(size - 1)]
        down = [(j, i) for i, j in up]
        last = lax.slice_in_dim(shard, length - width, length, axis=dim)
        first = lax.slice_in_dim(shard, 0, width, axis=dim)
        before = lax.ppermute(last, axis, up)
        after = lax.ppermute(first, axis, down)
        shard = jnp.concatenate([before, shard, after], axis=dim)
    return shard


def grouped_view(values):
    return values.reshape(
        values.shape[0], values.shape[1] * values.shape[2], GROUPS, values.shape[3] // GROUPS
    )


def group_sums(values):
    per = jnp.sum(values, axis=(1, 2))
    return jnp.sum(per.reshape(per.shape[0], GROUPS, per.shape[1] // GROUPS), axis=2)


def per_channel(stats, channels):
    wide = jnp.repeat(stats, channels // GROUPS, axis=1)
    return wide[:, None, None, :]


def widen_columns(values):
    return jnp.pad(values, ((0, 0), (0, 0), (1, 1), (0, 0)))


def plane_windows(plane, rows_here, columns, flip):
    taps = []
    for row_tap in range(3):
        for col_tap in range(3):
            r0 = 2 - row_tap if flip else row_tap
            c0 = 2 - col_tap if flip else col_tap
            window = plane[r0 : r0 + rows_here, c0 : c0 + columns]
            taps.append(window.reshape(rows_here * columns, 1, plane.shape[-1]))
    return jnp.concatenate(taps, axis=1)


def shards(latent, norm_gain, conv_weight, grad_out):
    frames_here, rows_here, columns, channels = latent.shape
    cell_count = lax.axis_size("rows") * rows_here * columns * (channels // GROUPS)
    full_weight = lax.all_gather(conv_weight, "tm", axis=1, tiled=True)
    after_one = shifted(grad_out, "tm", -1)
    after_two = shifted(grad_out, "tm", -2)
    padded_grad = with_halo(
        jnp.concatenate([grad_out, after_one, after_two], axis=0), (("rows", 1),), 1
    )
    padded_grad = widen_columns(padded_grad)
    latent_block = jnp.concatenate(
        [shifted(latent, "tm", 2), shifted(latent, "tm", 1), latent], axis=0
    )
    latent_padded = with_halo(latent_block, (("rows", 1),), 1)
    latent_wide = latent.astype(jnp.float32)
    block_wide = latent_block.astype(jnp.float32)
    average_block = lax.psum(group_sums(block_wide), "rows") / cell_count
    centred_block = block_wide - per_channel(average_block, channels)
    spread_block = lax.psum(group_sums(centred_block * centred_block), "rows") / cell_count
    inverse_block = lax.rsqrt(spread_block + epsilon)
    inverse = per_channel(inverse_block[2:], channels)
    normed = centred_block[2:] * inverse
    scaled = normed * norm_gain
    sigmoid_value = jax.nn.sigmoid(scaled)
    padded_average = per_channel(average_block, channels)
    padded_inverse = per_channel(inverse_block, channels)
    normed_padded = (latent_padded.astype(jnp.float32) - padded_average) * padded_inverse
    scaled_padded = normed_padded * norm_gain
    activated_padded = (scaled_padded * jax.nn.sigmoid(scaled_padded)).astype(jnp.bfloat16)
    frame_index = lax.axis_index("tm") * frames_here - 2 + lax.iota(jnp.int32, 3)
    row_index = lax.axis_index("rows") * rows_here - 1 + lax.iota(jnp.int32, rows_here + 2)
    inside = (frame_index[:, None] >= 0) & (row_index[None, :] >= 0)
    inside = inside & (row_index[None, :] < lax.axis_size("rows") * rows_here)
    padded = jnp.where(inside[:, :, None, None], activated_padded, jnp.zeros_like(activated_padded))
    padded = widen_columns(padded)
    positions = frames_here * rows_here * columns
    full_weight, padded, padded_grad = lax.optimization_barrier((full_weight, padded, padded_grad))
    head = plane_windows(padded[0], rows_here, columns, False)
    conv_head = jnp.dot(
        head.reshape(positions, 9 * channels),
        full_weight[0:9].reshape(9 * channels, channels),
        preferred_element_type=jnp.float32,
    )
    padded_grad, conv_head = lax.optimization_barrier((padded_grad, conv_head))
    grad_act = None
    for time_tap in range(3):
        part = full_weight[9 * time_tap : 9 * time_tap + 9]
        back = plane_windows(padded_grad[2 - time_tap], rows_here, columns, True)
        term = lax.dot_general(
            back, part, (((1, 2), (0, 2)), ((), ())), preferred_element_type=jnp.float32
        )
        grad_act = term if grad_act is None else grad_act + term
    grad_scaled = (
        grad_act.reshape(latent.shape) * sigmoid_value * (1.0 + scaled * (1.0 - sigmoid_value))
    )
    grad_normed = grad_scaled * norm_gain
    partial = jnp.stack([group_sums(grad_normed), group_sums(grad_normed * normed)])
    full_weight, padded, partial, conv_head = lax.optimization_barrier(
        (full_weight, padded, partial, conv_head)
    )
    size = lax.axis_size("rows")
    steps = []
    step = 1
    while step < size:
        steps.append(step)
        step *= 2
    total = partial
    conv_sum = conv_head
    for round_index in range(max(2, len(steps))):
        if round_index < len(steps):
            route = [(i, i ^ steps[round_index]) for i in range(size)]
            total = total + lax.ppermute(total, "rows", route)
        if round_index < 2:
            time_tap = round_index + 1
            part = full_weight[9 * time_tap : 9 * time_tap + 9]
            fwd = plane_windows(padded[time_tap], rows_here, columns, False)
            term = jnp.dot(
                fwd.reshape(positions, 9 * channels),
                part.reshape(9 * channels, channels),
                preferred_element_type=jnp.float32,
            )
            conv_sum = conv_sum + term
        total, conv_sum, padded = lax.optimization_barrier((total, conv_sum, padded))
    first_sum, second_sum = total
    refined = (latent_wide + conv_sum.reshape(latent.shape)).astype(jnp.bfloat16)
    first = first_sum / cell_count
    second = second_sum / cell_count
    first_wide = per_channel(first, channels)
    second_wide = per_channel(second, channels)
    grad_norm_part = (grad_normed - first_wide - normed * second_wide) * inverse
    grad_latent = grad_out.astype(jnp.float32) + grad_norm_part
    return (refined, grad_latent)


def solution(mesh):
    placed = (P("tm", "rows", None, None), P(), P(None, "tm", None), P("tm", "rows", None, None))
    return jax.shard_map(
        shards,
        mesh=mesh,
        in_specs=placed,
        out_specs=(P("tm", "rows", None, None), P("tm", "rows", None, None)),
        check_vma=False,
    )
```

```python
import jax
import jax.numpy as jnp
from jax import lax
from jax.sharding import PartitionSpec as P

GROUPS = 32


epsilon = 1e-06


def shifted(block, axis, distance):
    devices = range(lax.axis_size(axis))
    route = [(i - distance, i) for i in devices if i - distance in devices]
    return lax.ppermute(block, axis, route)


def with_halo(shard, sides, width):
    for axis, dim in sides:
        size, length = (lax.axis_size(axis), shard.shape[dim])
        up = [(i, (i + 1) % size) for i in range(size - 1)]
        down = [(j, i) for i, j in up]
        last = lax.slice_in_dim(shard, length - width, length, axis=dim)
        first = lax.slice_in_dim(shard, 0, width, axis=dim)
        before = lax.ppermute(last, axis, up)
        after = lax.ppermute(first, axis, down)
        shard = jnp.concatenate([before, shard, after], axis=dim)
    return shard


def grouped_view(values):
    return values.reshape(
        values.shape[0], values.shape[1] * values.shape[2], GROUPS, values.shape[3] // GROUPS
    )


def group_sums(values):
    per = jnp.sum(values, axis=(1, 2))
    return jnp.sum(per.reshape(per.shape[0], GROUPS, per.shape[1] // GROUPS), axis=2)


def per_channel(stats, channels):
    wide = jnp.repeat(stats, channels // GROUPS, axis=1)
    return wide[:, None, None, :]


def widen_columns(values):
    return jnp.pad(values, ((0, 0), (0, 0), (1, 1), (0, 0)))


def plane_windows(plane, rows_here, columns, flip):
    taps = []
    for row_tap in range(3):
        for col_tap in range(3):
            r0 = 2 - row_tap if flip else row_tap
            c0 = 2 - col_tap if flip else col_tap
            window = plane[r0 : r0 + rows_here, c0 : c0 + columns]
            taps.append(window.reshape(rows_here * columns, 1, plane.shape[-1]))
    return jnp.concatenate(taps, axis=1)


def shards(latent, norm_gain, conv_weight, grad_out):
    frames_here, rows_here, columns, channels = latent.shape
    cell_count = lax.axis_size("rows") * rows_here * columns * (channels // GROUPS)
    full_weight = lax.all_gather(conv_weight, "tm", axis=1, tiled=True)
    after_one = shifted(grad_out, "tm", -1)
    after_two = shifted(grad_out, "tm", -2)
    padded_grad = with_halo(
        jnp.concatenate([grad_out, after_one, after_two], axis=0), (("rows", 1),), 1
    )
    padded_grad = widen_columns(padded_grad)
    latent_block = jnp.concatenate(
        [shifted(latent, "tm", 2), shifted(latent, "tm", 1), latent], axis=0
    )
    latent_padded = with_halo(latent_block, (("rows", 1),), 1)
    latent_wide = latent.astype(jnp.float32)
    block_wide = latent_block.astype(jnp.float32)
    average_block = lax.psum(group_sums(block_wide), "rows") / cell_count
    centred_block = block_wide - per_channel(average_block, channels)
    spread_block = lax.psum(group_sums(centred_block * centred_block), "rows") / cell_count
    inverse_block = lax.rsqrt(spread_block + epsilon)
    inverse = per_channel(inverse_block[2:], channels)
    normed = centred_block[2:] * inverse
    scaled = normed * norm_gain
    sigmoid_value = jax.nn.sigmoid(scaled)
    padded_average = per_channel(average_block, channels)
    padded_inverse = per_channel(inverse_block, channels)
    normed_padded = (latent_padded.astype(jnp.float32) - padded_average) * padded_inverse
    scaled_padded = normed_padded * norm_gain
    activated_padded = (scaled_padded * jax.nn.sigmoid(scaled_padded)).astype(jnp.bfloat16)
    frame_index = lax.axis_index("tm") * frames_here - 2 + lax.iota(jnp.int32, 3)
    row_index = lax.axis_index("rows") * rows_here - 1 + lax.iota(jnp.int32, rows_here + 2)
    inside = (frame_index[:, None] >= 0) & (row_index[None, :] >= 0)
    inside = inside & (row_index[None, :] < lax.axis_size("rows") * rows_here)
    padded = jnp.where(inside[:, :, None, None], activated_padded, jnp.zeros_like(activated_padded))
    padded = widen_columns(padded)
    positions = frames_here * rows_here * columns
    full_weight, padded, padded_grad = lax.optimization_barrier((full_weight, padded, padded_grad))
    grad_act = None
    for time_tap in range(3):
        part = full_weight[9 * time_tap : 9 * time_tap + 9]
        back = plane_windows(padded_grad[2 - time_tap], rows_here, columns, True)
        term = lax.dot_general(
            back, part, (((1, 2), (0, 2)), ((), ())), preferred_element_type=jnp.float32
        )
        grad_act = term if grad_act is None else grad_act + term
    grad_scaled = (
        grad_act.reshape(latent.shape) * sigmoid_value * (1.0 + scaled * (1.0 - sigmoid_value))
    )
    grad_normed = grad_scaled * norm_gain
    partial = jnp.stack([group_sums(grad_normed), group_sums(grad_normed * normed)])
    full_weight, padded, partial = lax.optimization_barrier((full_weight, padded, partial))
    size = lax.axis_size("rows")
    steps = []
    step = 1
    while step < size:
        steps.append(step)
        step *= 2
    steps = steps[::-1]
    total = partial
    conv_sum = None
    for time_tap in range(max(3, len(steps))):
        if time_tap < len(steps):
            route = [(i, i ^ steps[time_tap]) for i in range(size)]
            total = total + lax.ppermute(total, "rows", route)
        if time_tap < 3:
            part = full_weight[9 * time_tap : 9 * time_tap + 9]
            fwd = plane_windows(padded[time_tap], rows_here, columns, False)
            term = jnp.dot(
                fwd.reshape(positions, 9 * channels),
                part.reshape(9 * channels, channels),
                preferred_element_type=jnp.float32,
            )
            conv_sum = term if conv_sum is None else conv_sum + term
        total, conv_sum, padded = lax.optimization_barrier((total, conv_sum, padded))
    first_sum, second_sum = total
    refined = (latent_wide + conv_sum.reshape(latent.shape)).astype(jnp.bfloat16)
    first = first_sum / cell_count
    second = second_sum / cell_count
    first_wide = per_channel(first, channels)
    second_wide = per_channel(second, channels)
    grad_norm_part = (grad_normed - first_wide - normed * second_wide) * inverse
    grad_latent = grad_out.astype(jnp.float32) + grad_norm_part
    return (refined, grad_latent)


def solution(mesh):
    placed = (P("tm", "rows", None, None), P(), P(None, "tm", None), P("tm", "rows", None, None))
    return jax.shard_map(
        shards,
        mesh=mesh,
        in_specs=placed,
        out_specs=(P("tm", "rows", None, None), P("tm", "rows", None, None)),
        check_vma=False,
    )
```
